256 devices in a mesh: leaf: 64 (over y_lo, z, x), win: 4 (over y_hi, core).
Axes of the slice: x: 4, y: 4 (y_hi: 2, y_lo: 2; y = y_hi * 2 + y_lo), z: 8, core: 2. Of those that a mesh axis runs over, the one named last changes fastest.
Arguments:
- blocks: float32 [65536, 256], P(('win', 'leaf')), parts along dimension 0, may hold values from 0 to 3, as said below
- factors: float32 [65536, 4, 256], P(('win', 'leaf')), parts along dimension 0, may hold values from -6 to 6
- targets: float32 [65536, 128], P(('win', 'leaf')), parts along dimension 0, may hold values from -6 to 6
Outputs:
- coarse: float32 [65536, 256], P(('win', 'leaf')), parts along dimension 0
- solution: float32 [65536, 128], P(('win', 'leaf')), parts along dimension 0
The draws below stay inside these ranges and needn't reach their ends.
There are 4 independent parts, one for each index of `win`. The reference program is written for one: setup_inputs(seed, part) draws one part's arguments, and reference() takes and returns one part's arrays. A program takes and returns all parts, laid end to end along the dimension named above; each array names one. Nothing has to cross between parts.
Inputs may be any that keep to these rules, and one draw needn't show every extreme that they name: `blocks`: every 256 x 256 block is symmetric positive definite.
All inputs are finite; a program needn't handle non-finite values.
Results may differ from the reference program's by a relative error of at most 0.0001.
Values sent between devices are 32-bit elements; how exact they have to be, the bound alone decides.
No kernel may reach another device: no remote copies, remote signals or barrier semaphores. Data moves between devices by JAX's collectives and lax.ppermute only.
A program may use at most 64 MiB of HBM per device.

```python
import jax
import jax.numpy as jnp
from jax import lax

ROWS_DEV = 256
COUPLING = 256
NRHS = 128
LEVELS = 3
ROWS = 16384


def draw_blocks(key, part):
    count = ROWS // ROWS_DEV
    keys = jax.random.split(jax.random.fold_in(key, 11), 3)
    jitter = jax.random.uniform(keys[0], (count, ROWS_DEV, 2), jnp.float32, -1.0, 1.0)
    amp_raw = jax.random.uniform(keys[1], (count, ROWS_DEV), jnp.float32, -1.0, 1.0)
    nug_raw = jax.random.uniform(keys[2], (count, ROWS_DEV), jnp.float32, 0.0, 1.0)
    length = 2.5
    amplitude = jnp.exp(0.3 * amp_raw)
    nugget = 0.2 + 0.3 * nug_raw
    shake = 0.35
    position = jnp.arange(ROWS_DEV, dtype=jnp.int32)
    grid_row = (position // 16).astype(jnp.float32)
    grid_col = (position % 16).astype(jnp.float32)
    point_x = grid_row[None, :] + shake * jitter[:, :, 0]
    point_y = grid_col[None, :] + shake * jitter[:, :, 1]
    delta_x = point_x[:, :, None] - point_x[:, None, :]
    delta_y = point_y[:, :, None] - point_y[:, None, :]
    distance = jnp.sqrt(delta_x * delta_x + delta_y * delta_y)
    kernel = amplitude[:, :, None] * amplitude[:, None, :] * jnp.exp(-distance / length)
    on_diag = position[:, None] == position[None, :]
    block = kernel + jnp.where(on_diag[None], nugget[:, :, None], 0.0)
    return block.reshape(ROWS, ROWS_DEV).astype(jnp.float32)


def steps_of(own_key, shape, cuts, least, high):
    def one(axis_at, parts):
        steps = jax.random.uniform(jax.random.fold_in(jax.random.fold_in(own_key, 6), axis_at), (parts,), jnp.float32, least / len(cuts), high / len(cuts))
        return jnp.repeat(jnp.exp(steps), shape[axis_at] // parts).reshape((-1,) + (1,) * (len(shape) - axis_at - 1))

    loudness = one(*cuts[0])
    for cut in cuts[1:]:
        loudness = loudness * one(*cut)
    return loudness


def centred(stream_key, dims, scale, limit, cuts=(), kind=jnp.bfloat16):
    drawn = scale * jax.random.normal(stream_key, dims, jnp.float32)
    if cuts:
        drawn = drawn * steps_of(stream_key, dims, cuts, -0.22, 0.18)
    return jnp.clip(drawn, -limit, limit).astype(kind)


def setup_inputs(seed: int = 0, part: int = 0) -> dict:
    seeds = jax.random.split(jax.random.key(seed), 4)
    part_keys = jax.random.split(jax.random.fold_in(seeds[3], part), 4)
    blocks = draw_blocks(jax.random.fold_in(jax.random.fold_in(seeds[3], part), 71), part)
    factors = centred(part_keys[1], (ROWS, LEVELS + 1, COUPLING), 1.0, 6.0, ((0, 64),), jnp.float32)
    targets = centred(part_keys[2], (ROWS, NRHS), 1.0, 6.0, ((0, 64),), jnp.float32)
    return dict(blocks=blocks, factors=factors, targets=targets)


def leaf_solve(pair):
    block, columns = pair
    lower = jnp.linalg.cholesky(block)
    return jax.scipy.linalg.cho_solve((lower, True), columns)

def coupling_solve(pair):
    coupling, right = pair
    lower = jnp.linalg.cholesky(coupling)
    return jax.scipy.linalg.cho_solve((lower, True), right)

def reference(blocks, factors, targets):
    count = ROWS // ROWS_DEV
    width = COUPLING
    columns = jnp.concatenate([factors.reshape(ROWS, (LEVELS + 1) * width), targets], axis=1)
    solved = lax.map(leaf_solve, (blocks.reshape(count, ROWS_DEV, ROWS_DEV), columns.reshape(count, ROWS_DEV, -1)))
    basis_all = factors.reshape(count, ROWS_DEV, LEVELS + 1, width)
    identity = jnp.eye(width, dtype=jnp.float32)
    for height in range(LEVELS):
        group_size = 2 ** (height + 1)
        nodes = count // group_size
        weight = 1.0 / (group_size * ROWS_DEV)
        node_rows = solved.reshape(nodes, group_size * ROWS_DEV, -1)
        basis_rows = basis_all[:, :, height, :].reshape(nodes, group_size * ROWS_DEV, width)
        panels = jnp.einsum('nrk,nrc->nkc', basis_rows, node_rows, precision=lax.Precision.HIGHEST)
        couplings = identity[None] + weight * panels[:, :, :width]
        update = lax.map(coupling_solve, (couplings, weight * panels[:, :, width:]))
        remaining = node_rows[:, :, width:] - jnp.einsum('nrk,nkc->nrc', node_rows[:, :, :width], update, precision=lax.Precision.HIGHEST)
        solved = remaining.reshape(count, ROWS_DEV, -1)
    final = solved.reshape(ROWS, -1)
    return (final[:, :width], final[:, width:])
```

```python
import jax
import jax.numpy as jnp
from jax import lax
from jax.sharding import PartitionSpec as P

LEVELS = 3
HIGH = lax.Precision.HIGHEST


def from_partner(array, axis, apart):
    return lax.ppermute(array, axis, [(i, i ^ 1 << apart) for i in range(lax.axis_size(axis))])


def cross_rows(left, right):
    return lax.dot_general(
        left,
        right,
        (((0,), (0,)), ((), ())),
        precision=HIGH,
        preferred_element_type=jnp.float32,
    )


def mm(left, right):
    return jnp.dot(left, right, precision=HIGH, preferred_element_type=jnp.float32)


def mm_t(left, right):
    return lax.dot_general(
        left, right, (((1,), (1,)), ((), ())), precision=HIGH, preferred_element_type=jnp.float32
    )


def tri_inverse(lower):
    eye = jnp.eye(lower.shape[0], dtype=lower.dtype)
    return lax.linalg.triangular_solve(lower, eye, left_side=True, lower=True)


def factor(matrix):
    matrix = (matrix + matrix.T) * 0.5
    half = matrix.shape[0] // 2
    a11 = matrix[:half, :half]
    a21 = matrix[half:, :half]
    a22 = matrix[half:, half:]
    l11 = jnp.tril(lax.linalg.cholesky(a11, symmetrize_input=False))
    w1 = jnp.tril(tri_inverse(l11))
    l21 = mm_t(a21, w1)
    schur = a22 - mm_t(l21, l21)
    l22 = jnp.tril(lax.linalg.cholesky(schur, symmetrize_input=False))
    w2 = jnp.tril(tri_inverse(l22))
    return w1, l21, w2


def solve(parts, right):
    w1, l21, w2 = parts
    half = w1.shape[0]
    y1 = mm(w1, right[:half])
    y2 = mm(w2, right[half:] - mm(l21, y1))
    x2 = cross_rows(w2, y2)
    x1 = cross_rows(w1, y1 - cross_rows(l21, x2))
    return jnp.concatenate([x1, x2], axis=0)


def shards(blocks, factors, targets):
    block_rows = blocks.shape[0]
    coupling = factors.shape[2]
    columns = jnp.concatenate([factors.reshape(block_rows, -1), targets], axis=1)
    solved = solve(factor(blocks), columns)
    identity = jnp.eye(coupling, dtype=jnp.float32)
    leaf_index = lax.axis_index("leaf")
    for height in range(LEVELS):
        group_size = 2 ** (height + 1)
        weight = 1.0 / (group_size * block_rows)
        basis_cols = factors[:, height, :]
        leading = solved[:, :coupling]
        remaining = solved[:, coupling:]
        gram = cross_rows(basis_cols, leading)
        pieces = cross_rows(basis_cols, remaining)
        for which_bit in range(height + 1):
            gram = gram + from_partner(gram, "leaf", which_bit)
        for which_bit in range(height + 1):
            half_cols = pieces.shape[1] // 2
            lower_half = pieces[:, :half_cols]
            upper_half = pieces[:, half_cols:]
            is_upper = leaf_index >> which_bit & 1 == 1
            outgoing = jnp.where(is_upper, lower_half, upper_half)
            kept = jnp.where(is_upper, upper_half, lower_half)
            pieces = kept + from_partner(outgoing, "leaf", which_bit)
        update = solve(factor(identity + weight * gram), weight * pieces)
        for which_bit in reversed(range(height + 1)):
            partner = from_partner(update, "leaf", which_bit)
            is_upper = leaf_index >> which_bit & 1 == 1
            update = jnp.where(
                is_upper,
                jnp.concatenate([partner, update], axis=1),
                jnp.concatenate([update, partner], axis=1),
            )
        solved = remaining - mm(leading, update)
    return (solved[:, :coupling], solved[:, coupling:])


def solution(mesh):
    placed = (P(("win", "leaf"), None), P(("win", "leaf"), None, None), P(("win", "leaf"), None))
    return jax.shard_map(
        shards,
        mesh=mesh,
        in_specs=placed,
        out_specs=(P(("win", "leaf"), None), P(("win", "leaf"), None)),
        check_vma=False,
    )
```

```python
import jax
import jax.numpy as jnp
from jax import lax
from jax.sharding import PartitionSpec as P

LEVELS = 3
HIGH = lax.Precision.HIGHEST


def from_partner(array, axis, apart):
    return lax.ppermute(array, axis, [(i, i ^ 1 << apart) for i in range(lax.axis_size(axis))])


def node_sum(array, height):
    for which_bit in range(height + 1):
        array = array + from_partner(array, "leaf", which_bit)
    return array


def cross_rows(left, right):
    return lax.dot_general(
        left,
        right,
        (((0,), (0,)), ((), ())),
        precision=HIGH,
        preferred_element_type=jnp.float32,
    )


def mm(left, right):
    return jnp.dot(left, right, precision=HIGH, preferred_element_type=jnp.float32)


def mm_t(left, right):
    return lax.dot_general(
        left, right, (((1,), (1,)), ((), ())), precision=HIGH, preferred_element_type=jnp.float32
    )


def tri_inverse(lower):
    eye = jnp.eye(lower.shape[0], dtype=lower.dtype)
    return lax.linalg.triangular_solve(lower, eye, left_side=True, lower=True)


def factor(matrix):
    matrix = (matrix + matrix.T) * 0.5
    half = matrix.shape[0] // 2
    a11 = matrix[:half, :half]
    a21 = matrix[half:, :half]
    a22 = matrix[half:, half:]
    l11 = jnp.tril(lax.linalg.cholesky(a11, symmetrize_input=False))
    w1 = jnp.tril(tri_inverse(l11))
    l21 = mm_t(a21, w1)
    schur = a22 - mm_t(l21, l21)
    l22 = jnp.tril(lax.linalg.cholesky(schur, symmetrize_input=False))
    w2 = jnp.tril(tri_inverse(l22))
    return w1, l21, w2


def solve(parts, right):
    w1, l21, w2 = parts
    half = w1.shape[0]
    y1 = mm(w1, right[:half])
    y2 = mm(w2, right[half:] - mm(l21, y1))
    x2 = cross_rows(w2, y2)
    x1 = cross_rows(w1, y1 - cross_rows(l21, x2))
    return jnp.concatenate([x1, x2], axis=0)


def shards(blocks, factors, targets):
    block_rows = blocks.shape[0]
    coupling = factors.shape[2]
    columns = jnp.concatenate([factors.reshape(block_rows, -1), targets], axis=1)
    solved = solve(factor(blocks), columns)
    identity = jnp.eye(coupling, dtype=jnp.float32)
    for height in range(LEVELS):
        group_size = 2 ** (height + 1)
        weight = 1.0 / (group_size * block_rows)
        basis_cols = factors[:, height, :]
        leading = solved[:, :coupling]
        remaining = solved[:, coupling:]
        gram = node_sum(cross_rows(basis_cols, leading), height)
        pieces = node_sum(cross_rows(basis_cols, remaining), height)
        update = solve(factor(identity + weight * gram), weight * pieces)
        solved = remaining - mm(leading, update)
    return (solved[:, :coupling], solved[:, coupling:])


def solution(mesh):
    placed = (P(("win", "leaf"), None), P(("win", "leaf"), None, None), P(("win", "leaf"), None))
    return jax.shard_map(
        shards,
        mesh=mesh,
        in_specs=placed,
        out_specs=(P(("win", "leaf"), None), P(("win", "leaf"), None)),
        check_vma=False,
    )
```

```python
import jax
import jax.numpy as jnp
from jax import lax
from jax.sharding import PartitionSpec as P

LEVELS = 3
HIGH = lax.Precision.HIGHEST


def from_partner(array, axis, apart):
    return lax.ppermute(array, axis, [(i, i ^ 1 << apart) for i in range(lax.axis_size(axis))])


def node_sum(array, height):
    for which_bit in range(height + 1):
        array = array + from_partner(array, "leaf", which_bit)
    return array


def cross_rows(left, right):
    return lax.dot_general(
        left,
        right,
        (((0,), (0,)), ((), ())),
        precision=HIGH,
        preferred_element_type=jnp.float32,
    )


def mm(left, right):
    return jnp.dot(left, right, precision=HIGH, preferred_element_type=jnp.float32)


def mm_t(left, right):
    return lax.dot_general(
        left, right, (((1,), (1,)), ((), ())), precision=HIGH, preferred_element_type=jnp.float32
    )


def tri_inverse(lower):
    eye = jnp.eye(lower.shape[0], dtype=lower.dtype)
    return lax.linalg.triangular_solve(lower, eye, left_side=True, lower=True)


def factor(matrix):
    matrix = (matrix + matrix.T) * 0.5
    half = matrix.shape[0] // 2
    a11 = matrix[:half, :half]
    a21 = matrix[half:, :half]
    a22 = matrix[half:, half:]
    l11 = lax.linalg.cholesky(a11, symmetrize_input=False)
    l11 = jnp.tril(l11)
    w1 = jnp.tril(tri_inverse(l11))
    l21 = mm_t(a21, w1)
    schur = a22 - mm_t(l21, l21)
    l22 = lax.linalg.cholesky(schur, symmetrize_input=False)
    l22 = jnp.tril(l22)
    w2 = jnp.tril(tri_inverse(l22))
    return w1, l21, w2


def solve(parts, right):
    w1, l21, w2 = parts
    half = w1.shape[0]
    y1 = mm(w1, right[:half])
    y2 = mm(w2, right[half:] - mm(l21, y1))
    x2 = cross_rows(w2, y2)
    x1 = cross_rows(w1, y1 - cross_rows(l21, x2))
    return jnp.concatenate([x1, x2], axis=0)


def level_step(height, blocks_rows, factors, solved, gram, identity):
    width = factors.shape[2]
    weight = 1.0 / (2 ** (height + 1) * blocks_rows)
    basis = factors[:, height, :]
    leading = solved[:, :width]
    remaining = solved[:, width:]
    parts = factor(identity + weight * gram)
    if height == LEVELS - 1:
        panel = node_sum(cross_rows(basis, remaining), height)
        update = solve(parts, weight * panel)
    else:
        following = factors[:, height + 1, :]
        head = remaining[:, :width]
        projections = jnp.concatenate(
            [cross_rows(basis, head), cross_rows(following, leading), cross_rows(following, head)],
            axis=1,
        )
        early = node_sum(projections, height)
        rest = node_sum(cross_rows(basis, remaining[:, width:]), height)
        first = solve(parts, weight * early[:, :width])
        update = jnp.concatenate([first, solve(parts, weight * rest)], axis=1)
        child = early[:, 2 * width :] - mm(early[:, width : 2 * width], first)
        gram = child + from_partner(child, "leaf", height + 1)
    solved = remaining - mm(leading, update)
    return solved, gram


def shards(blocks, factors, targets):
    block_rows = blocks.shape[0]
    width = factors.shape[2]
    columns = jnp.concatenate([factors.reshape(block_rows, -1), targets], axis=1)
    solved = solve(factor(blocks), columns)
    identity = jnp.eye(width, dtype=jnp.float32)
    gram = node_sum(cross_rows(factors[:, 0, :], solved[:, :width]), 0)
    for height in range(LEVELS):
        solved, gram = level_step(height, block_rows, factors, solved, gram, identity)
    return (solved[:, :width], solved[:, width:])


def solution(mesh):
    placed = (P(("win", "leaf"), None), P(("win", "leaf"), None, None), P(("win", "leaf"), None))
    return jax.shard_map(
        shards,
        mesh=mesh,
        in_specs=placed,
        out_specs=(P(("win", "leaf"), None), P(("win", "leaf"), None)),
        check_vma=False,
    )
```

```python
import jax
import jax.numpy as jnp
from jax import lax
from jax.sharding import PartitionSpec as P

LEVELS = 3
HIGH = lax.Precision.HIGHEST


def from_partner(array, axis, apart):
    return lax.ppermute(array, axis, [(i, i ^ 1 << apart) for i in range(lax.axis_size(axis))])


def node_sum(array, height):
    for which_bit in range(height + 1):
        array = array + from_partner(array, "leaf", which_bit)
    return array


def cross_rows(left, right):
    return lax.dot_general(
        left,
        right,
        (((0,), (0,)), ((), ())),
        precision=HIGH,
        preferred_element_type=jnp.float32,
    )


def mm(left, right):
    return jnp.dot(left, right, precision=HIGH, preferred_element_type=jnp.float32)


def mm_t(left, right):
    return lax.dot_general(
        left, right, (((1,), (1,)), ((), ())), precision=HIGH, preferred_element_type=jnp.float32
    )


def tri_inverse(lower):
    eye = jnp.eye(lower.shape[0], dtype=lower.dtype)
    return lax.linalg.triangular_solve(lower, eye, left_side=True, lower=True)


def factor(matrix):
    matrix = (matrix + matrix.T) * 0.5
    half = matrix.shape[0] // 2
    a11 = matrix[:half, :half]
    a21 = matrix[half:, :half]
    a22 = matrix[half:, half:]
    l11 = lax.linalg.cholesky(a11, symmetrize_input=False)
    l11 = jnp.tril(l11)
    w1 = jnp.tril(tri_inverse(l11))
    l21 = mm_t(a21, w1)
    schur = a22 - mm_t(l21, l21)
    l22 = lax.linalg.cholesky(schur, symmetrize_input=False)
    l22 = jnp.tril(l22)
    w2 = jnp.tril(tri_inverse(l22))
    return w1, l21, w2


def solve(parts, right):
    w1, l21, w2 = parts
    half = w1.shape[0]
    y1 = mm(w1, right[:half])
    y2 = mm(w2, right[half:] - mm(l21, y1))
    x2 = cross_rows(w2, y2)
    x1 = cross_rows(w1, y1 - cross_rows(l21, x2))
    return jnp.concatenate([x1, x2], axis=0)


def level_step(height, blocks_rows, factors, solved, gram, identity):
    width = factors.shape[2]
    weight = 1.0 / (2 ** (height + 1) * blocks_rows)
    basis = factors[:, height, :]
    leading = solved[:, :width]
    remaining = solved[:, width:]
    parts = factor(identity + weight * gram)
    if height == LEVELS - 1:
        panel = node_sum(cross_rows(basis, remaining), height)
        update = solve(parts, weight * panel)
    else:
        following = factors[:, height + 1, :]
        head = remaining[:, :width]
        projections = jnp.concatenate(
            [cross_rows(basis, head), cross_rows(following, leading), cross_rows(following, head)],
            axis=1,
        )
        early = node_sum(projections, height)
        rest = node_sum(cross_rows(basis, remaining[:, width:]), height)
        first = solve(parts, weight * early[:, :width])
        child = early[:, 2 * width :] - mm(early[:, width : 2 * width], first)
        gram = child + from_partner(child, "leaf", height + 1)
        update = jnp.concatenate([first, solve(parts, weight * rest)], axis=1)
    solved = remaining - mm(leading, update)
    return solved, gram


def shards(blocks, factors, targets):
    block_rows = blocks.shape[0]
    width = factors.shape[2]
    leaf_parts = factor(blocks)
    leading = solve(leaf_parts, factors[:, 0, :])
    gram = node_sum(cross_rows(factors[:, 0, :], leading), 0)
    others = jnp.concatenate([factors[:, 1:, :].reshape(block_rows, -1), targets], axis=1)
    solved = jnp.concatenate([leading, solve(leaf_parts, others)], axis=1)
    identity = jnp.eye(width, dtype=jnp.float32)
    for height in range(LEVELS):
        solved, gram = level_step(height, block_rows, factors, solved, gram, identity)
    return (solved[:, :width], solved[:, width:])


def solution(mesh):
    placed = (P(("win", "leaf"), None), P(("win", "leaf"), None, None), P(("win", "leaf"), None))
    return jax.shard_map(
        shards,
        mesh=mesh,
        in_specs=placed,
        out_specs=(P(("win", "leaf"), None), P(("win", "leaf"), None)),
        check_vma=False,
    )
```

```python
import jax
import jax.numpy as jnp
from jax import lax
from jax.sharding import PartitionSpec as P

LEVELS = 3
HIGH = lax.Precision.HIGHEST


def from_partner(array, axis, apart):
    return lax.ppermute(array, axis, [(i, i ^ 1 << apart) for i in range(lax.axis_size(axis))])


def node_sum(array, height):
    for which_bit in range(height + 1):
        array = array + from_partner(array, "leaf", which_bit)
    return array


def cross_rows(left, right):
    return lax.dot_general(
        left,
        right,
        (((0,), (0,)), ((), ())),
        precision=HIGH,
        preferred_element_type=jnp.float32,
    )


def mm(left, right):
    return jnp.dot(left, right, precision=HIGH, preferred_element_type=jnp.float32)


def mm_t(left, right):
    return lax.dot_general(
        left, right, (((1,), (1,)), ((), ())), precision=HIGH, preferred_element_type=jnp.float32
    )


def tri_inverse(lower):
    eye = jnp.eye(lower.shape[0], dtype=lower.dtype)
    return lax.linalg.triangular_solve(lower, eye, left_side=True, lower=True)


def factor(matrix, symmetrize=True):
    if symmetrize:
        matrix = (matrix + matrix.T) * 0.5
    half = matrix.shape[0] // 2
    a11 = matrix[:half, :half]
    a21 = matrix[half:, :half]
    a22 = matrix[half:, half:]
    l11 = lax.linalg.cholesky(a11, symmetrize_input=False)
    l11 = jnp.tril(l11)
    w1 = jnp.tril(tri_inverse(l11))
    l21 = mm_t(a21, w1)
    schur = a22 - mm_t(l21, l21)
    l22 = lax.linalg.cholesky(schur, symmetrize_input=False)
    l22 = jnp.tril(l22)
    w2 = jnp.tril(tri_inverse(l22))
    return w1, l21, w2


def solve(parts, right):
    w1, l21, w2 = parts
    half = w1.shape[0]
    y1 = mm(w1, right[:half])
    y2 = mm(w2, right[half:] - mm(l21, y1))
    x2 = cross_rows(w2, y2)
    x1 = cross_rows(w1, y1 - cross_rows(l21, x2))
    return jnp.concatenate([x1, x2], axis=0)


def level_step(height, blocks_rows, factors, solved, gram, identity):
    width = factors.shape[2]
    weight = 1.0 / (2 ** (height + 1) * blocks_rows)
    basis = factors[:, height, :]
    leading = solved[:, :width]
    remaining = solved[:, width:]
    parts = factor(identity + weight * gram)
    if height == LEVELS - 1:
        panel = node_sum(cross_rows(basis, remaining), height)
        update = solve(parts, weight * panel)
    else:
        following = factors[:, height + 1, :]
        head = remaining[:, :width]
        projections = jnp.concatenate(
            [
                cross_rows(basis, head),
                cross_rows(following, leading),
                cross_rows(following, head),
                cross_rows(basis, remaining[:, width:]),
            ],
            axis=1,
        )
        panel = node_sum(projections, height)
        first = solve(parts, weight * panel[:, :width])
        child = panel[:, 2 * width : 3 * width] - mm(panel[:, width : 2 * width], first)
        gram = child + from_partner(child, "leaf", height + 1)
        update = jnp.concatenate([first, solve(parts, weight * panel[:, 3 * width :])], axis=1)
    solved = remaining - mm(leading, update)
    return solved, gram


def shards(blocks, factors, targets):
    block_rows = blocks.shape[0]
    width = factors.shape[2]
    leaf_parts = factor(blocks, symmetrize=False)
    leading = solve(leaf_parts, factors[:, 0, :])
    gram = node_sum(cross_rows(factors[:, 0, :], leading), 0)
    others = jnp.concatenate([factors[:, 1:, :].reshape(block_rows, -1), targets], axis=1)
    solved = jnp.concatenate([leading, solve(leaf_parts, others)], axis=1)
    identity = jnp.eye(width, dtype=jnp.float32)
    for height in range(LEVELS):
        solved, gram = level_step(height, block_rows, factors, solved, gram, identity)
    return (solved[:, :width], solved[:, width:])


def solution(mesh):
    placed = (P(("win", "leaf"), None), P(("win", "leaf"), None, None), P(("win", "leaf"), None))
    return jax.shard_map(
        shards,
        mesh=mesh,
        in_specs=placed,
        out_specs=(P(("win", "leaf"), None), P(("win", "leaf"), None)),
        check_vma=False,
    )
```

```python
import jax
import jax.numpy as jnp
from jax import lax
from jax.sharding import PartitionSpec as P

LEVELS = 3
HIGH = lax.Precision.HIGHEST


def from_partner(array, axis, apart):
    return lax.ppermute(array, axis, [(i, i ^ 1 << apart) for i in range(lax.axis_size(axis))])


def node_sum(array, height):
    for which_bit in range(height + 1):
        array = array + from_partner(array, "leaf", which_bit)
    return array


def cross_rows(left, right):
    return lax.dot_general(
        left,
        right,
        (((0,), (0,)), ((), ())),
        precision=HIGH,
        preferred_element_type=jnp.float32,
    )


def mm(left, right):
    return jnp.dot(left, right, precision=HIGH, preferred_element_type=jnp.float32)


def mm_t(left, right):
    return lax.dot_general(
        left, right, (((1,), (1,)), ((), ())), precision=HIGH, preferred_element_type=jnp.float32
    )


def batched(left, right):
    return jnp.einsum("bij,bjk->bik", left, right, precision=HIGH, preferred_element_type=jnp.float32)


def diagonal_blocks(matrix, size):
    count = matrix.shape[0] // size
    tiles = matrix.reshape(count, size, count, size)
    mask = jnp.eye(count, dtype=matrix.dtype)[:, None, :, None]
    return jnp.sum(tiles * mask, axis=2)


def tri_inverse(lower, base=8):
    size = lower.shape[0]
    count = size // base
    blocks = diagonal_blocks(lower, base)
    rows = []
    for i in range(base):
        unit = (jnp.arange(base) == i).astype(lower.dtype)
        acc = jnp.broadcast_to(unit, (count, base))
        for k in range(i):
            acc = acc - blocks[:, i, k][:, None] * rows[k]
        rows.append(acc / blocks[:, i, i][:, None])
    inverse = jnp.stack(rows, axis=1)
    step = base
    while step < size:
        first = inverse[0::2]
        second = inverse[1::2]
        below = diagonal_blocks(lower, 2 * step)[:, step:, :step]
        corner = -batched(batched(second, below), first)
        top = jnp.concatenate([first, jnp.zeros_like(first)], axis=2)
        bottom = jnp.concatenate([corner, second], axis=2)
        inverse = jnp.concatenate([top, bottom], axis=1)
        step *= 2
    return inverse[0]


def factor(matrix, symmetrize=True):
    if symmetrize:
        matrix = (matrix + matrix.T) * 0.5
    half = matrix.shape[0] // 2
    a11 = matrix[:half, :half]
    a21 = matrix[half:, :half]
    a22 = matrix[half:, half:]
    l11 = lax.linalg.cholesky(a11, symmetrize_input=False)
    l11 = jnp.tril(l11)
    w1 = jnp.tril(tri_inverse(l11))
    l21 = mm_t(a21, w1)
    schur = a22 - mm_t(l21, l21)
    l22 = lax.linalg.cholesky(schur, symmetrize_input=False)
    l22 = jnp.tril(l22)
    w2 = jnp.tril(tri_inverse(l22))
    return w1, l21, w2


def solve(parts, right):
    w1, l21, w2 = parts
    half = w1.shape[0]
    y1 = mm(w1, right[:half])
    y2 = mm(w2, right[half:] - mm(l21, y1))
    x2 = cross_rows(w2, y2)
    x1 = cross_rows(w1, y1 - cross_rows(l21, x2))
    return jnp.concatenate([x1, x2], axis=0)


def level_step(height, blocks_rows, factors, solved, gram, identity):
    width = factors.shape[2]
    weight = 1.0 / (2 ** (height + 1) * blocks_rows)
    basis = factors[:, height, :]
    leading = solved[:, :width]
    remaining = solved[:, width:]
    parts = factor(identity + weight * gram)
    if height == LEVELS - 1:
        panel = node_sum(cross_rows(basis, remaining), height)
        update = solve(parts, weight * panel)
    else:
        following = factors[:, height + 1, :]
        head = remaining[:, :width]
        projections = jnp.concatenate(
            [
                cross_rows(basis, head),
                cross_rows(following, leading),
                cross_rows(following, head),
                cross_rows(basis, remaining[:, width:]),
            ],
            axis=1,
        )
        panel = node_sum(projections, height)
        first = solve(parts, weight * panel[:, :width])
        child = panel[:, 2 * width : 3 * width] - mm(panel[:, width : 2 * width], first)
        gram = child + from_partner(child, "leaf", height + 1)
        update = jnp.concatenate([first, solve(parts, weight * panel[:, 3 * width :])], axis=1)
    solved = remaining - mm(leading, update)
    return solved, gram


def shards(blocks, factors, targets):
    block_rows = blocks.shape[0]
    width = factors.shape[2]
    leaf_parts = factor(blocks, symmetrize=False)
    leading = solve(leaf_parts, factors[:, 0, :])
    gram = node_sum(cross_rows(factors[:, 0, :], leading), 0)
    others = jnp.concatenate([factors[:, 1:, :].reshape(block_rows, -1), targets], axis=1)
    solved = jnp.concatenate([leading, solve(leaf_parts, others)], axis=1)
    identity = jnp.eye(width, dtype=jnp.float32)
    for height in range(LEVELS):
        solved, gram = level_step(height, block_rows, factors, solved, gram, identity)
    return (solved[:, :width], solved[:, width:])


def solution(mesh):
    placed = (P(("win", "leaf"), None), P(("win", "leaf"), None, None), P(("win", "leaf"), None))
    return jax.shard_map(
        shards,
        mesh=mesh,
        in_specs=placed,
        out_specs=(P(("win", "leaf"), None), P(("win", "leaf"), None)),
        check_vma=False,
    )
```

```python
import jax
import jax.numpy as jnp
from jax import lax
from jax.sharding import PartitionSpec as P

LEVELS = 3
HIGH = lax.Precision.HIGHEST


def from_partner(array, axis, apart):
    return lax.ppermute(array, axis, [(i, i ^ 1 << apart) for i in range(lax.axis_size(axis))])


def node_sum(array, height):
    for which_bit in range(height + 1):
        array = array + from_partner(array, "leaf", which_bit)
    return array


def cross_rows(left, right):
    return lax.dot_general(
        left,
        right,
        (((0,), (0,)), ((), ())),
        precision=HIGH,
        preferred_element_type=jnp.float32,
    )


def mm(left, right):
    return jnp.dot(left, right, precision=HIGH, preferred_element_type=jnp.float32)


def mm_t(left, right):
    return lax.dot_general(
        left, right, (((1,), (1,)), ((), ())), precision=HIGH, preferred_element_type=jnp.float32
    )


def batched(left, right):
    return jnp.einsum("bij,bjk->bik", left, right, precision=HIGH, preferred_element_type=jnp.float32)


def tri_inverse(lower, base=8):
    size = lower.shape[0]
    count = size // base
    blocks = jnp.stack([lower[i * base : (i + 1) * base, i * base : (i + 1) * base] for i in range(count)])
    rows = []
    for i in range(base):
        unit = (jnp.arange(base) == i).astype(lower.dtype)
        acc = jnp.broadcast_to(unit, (count, base))
        for k in range(i):
            acc = acc - blocks[:, i, k][:, None] * rows[k]
        rows.append(acc / blocks[:, i, i][:, None])
    inverse = jnp.stack(rows, axis=1)
    step = base
    while step < size:
        pairs = size // (2 * step)
        first = inverse[0::2]
        second = inverse[1::2]
        below = jnp.stack(
            [lower[(2 * j + 1) * step : (2 * j + 2) * step, 2 * j * step : (2 * j + 1) * step] for j in range(pairs)]
        )
        corner = -batched(batched(second, below), first)
        top = jnp.concatenate([first, jnp.zeros_like(first)], axis=2)
        bottom = jnp.concatenate([corner, second], axis=2)
        inverse = jnp.concatenate([top, bottom], axis=1)
        step *= 2
    return inverse[0]


def factor(matrix, symmetrize=True):
    if symmetrize:
        matrix = (matrix + matrix.T) * 0.5
    half = matrix.shape[0] // 2
    a11 = matrix[:half, :half]
    a21 = matrix[half:, :half]
    a22 = matrix[half:, half:]
    l11 = lax.linalg.cholesky(a11, symmetrize_input=False)
    l11 = jnp.tril(l11)
    w1 = jnp.tril(tri_inverse(l11))
    l21 = mm_t(a21, w1)
    schur = a22 - mm_t(l21, l21)
    l22 = lax.linalg.cholesky(schur, symmetrize_input=False)
    l22 = jnp.tril(l22)
    w2 = jnp.tril(tri_inverse(l22))
    return w1, l21, w2


def solve(parts, right):
    w1, l21, w2 = parts
    half = w1.shape[0]
    y1 = mm(w1, right[:half])
    y2 = mm(w2, right[half:] - mm(l21, y1))
    x2 = cross_rows(w2, y2)
    x1 = cross_rows(w1, y1 - cross_rows(l21, x2))
    return jnp.concatenate([x1, x2], axis=0)


def level_step(height, blocks_rows, factors, solved, gram, identity):
    width = factors.shape[2]
    weight = 1.0 / (2 ** (height + 1) * blocks_rows)
    basis = factors[:, height, :]
    leading = solved[:, :width]
    remaining = solved[:, width:]
    parts = factor(identity + weight * gram)
    if height == LEVELS - 1:
        panel = node_sum(cross_rows(basis, remaining), height)
        update = solve(parts, weight * panel)
    else:
        following = factors[:, height + 1, :]
        head = remaining[:, :width]
        projections = jnp.concatenate(
            [
                cross_rows(basis, head),
                cross_rows(following, leading),
                cross_rows(following, head),
                cross_rows(basis, remaining[:, width:]),
            ],
            axis=1,
        )
        panel = node_sum(projections, height)
        first = solve(parts, weight * panel[:, :width])
        child = panel[:, 2 * width : 3 * width] - mm(panel[:, width : 2 * width], first)
        gram = child + from_partner(child, "leaf", height + 1)
        update = jnp.concatenate([first, solve(parts, weight * panel[:, 3 * width :])], axis=1)
    solved = remaining - mm(leading, update)
    return solved, gram


def shards(blocks, factors, targets):
    block_rows = blocks.shape[0]
    width = factors.shape[2]
    leaf_parts = factor(blocks, symmetrize=False)
    leading = solve(leaf_parts, factors[:, 0, :])
    gram = node_sum(cross_rows(factors[:, 0, :], leading), 0)
    others = jnp.concatenate([factors[:, 1:, :].reshape(block_rows, -1), targets], axis=1)
    solved = jnp.concatenate([leading, solve(leaf_parts, others)], axis=1)
    identity = jnp.eye(width, dtype=jnp.float32)
    for height in range(LEVELS):
        solved, gram = level_step(height, block_rows, factors, solved, gram, identity)
    return (solved[:, :width], solved[:, width:])


def solution(mesh):
    placed = (P(("win", "leaf"), None), P(("win", "leaf"), None, None), P(("win", "leaf"), None))
    return jax.shard_map(
        shards,
        mesh=mesh,
        in_specs=placed,
        out_specs=(P(("win", "leaf"), None), P(("win", "leaf"), None)),
        check_vma=False,
    )
```

```python
import jax
import jax.numpy as jnp
from jax import lax
from jax.sharding import PartitionSpec as P

LEVELS = 3
HIGH = lax.Precision.HIGHEST


def from_partner(array, axis, apart):
    return lax.ppermute(array, axis, [(i, i ^ 1 << apart) for i in range(lax.axis_size(axis))])


def node_sum(array, height, order=None):
    for which_bit in order if order is not None else range(height + 1):
        array = array + from_partner(array, "leaf", which_bit)
    return array


def cross_rows(left, right):
    return lax.dot_general(
        left,
        right,
        (((0,), (0,)), ((), ())),
        precision=HIGH,
        preferred_element_type=jnp.float32,
    )


def mm(left, right):
    return jnp.dot(left, right, precision=HIGH, preferred_element_type=jnp.float32)


def mm_t(left, right):
    return lax.dot_general(
        left, right, (((1,), (1,)), ((), ())), precision=HIGH, preferred_element_type=jnp.float32
    )


def batched(left, right):
    return jnp.einsum("bij,bjk->bik", left, right, precision=HIGH, preferred_element_type=jnp.float32)


def tri_inverse(lower, base=8):
    size = lower.shape[0]
    count = size // base
    blocks = jnp.stack([lower[i * base : (i + 1) * base, i * base : (i + 1) * base] for i in range(count)])
    rows = []
    for i in range(base):
        unit = (jnp.arange(base) == i).astype(lower.dtype)
        acc = jnp.broadcast_to(unit, (count, base))
        for k in range(i):
            acc = acc - blocks[:, i, k][:, None] * rows[k]
        rows.append(acc / blocks[:, i, i][:, None])
    inverse = jnp.stack(rows, axis=1)
    step = base
    while step < size:
        pairs = size // (2 * step)
        first = inverse[0::2]
        second = inverse[1::2]
        below = jnp.stack(
            [lower[(2 * j + 1) * step : (2 * j + 2) * step, 2 * j * step : (2 * j + 1) * step] for j in range(pairs)]
        )
        corner = -batched(batched(second, below), first)
        top = jnp.concatenate([first, jnp.zeros_like(first)], axis=2)
        bottom = jnp.concatenate([corner, second], axis=2)
        inverse = jnp.concatenate([top, bottom], axis=1)
        step *= 2
    return inverse[0]


def factor(matrix, symmetrize=True):
    if symmetrize:
        matrix = (matrix + matrix.T) * 0.5
    half = matrix.shape[0] // 2
    a11 = matrix[:half, :half]
    a21 = matrix[half:, :half]
    a22 = matrix[half:, half:]
    l11 = lax.linalg.cholesky(a11, symmetrize_input=False)
    l11 = jnp.tril(l11)
    w1 = jnp.tril(tri_inverse(l11))
    l21 = mm_t(a21, w1)
    schur = a22 - mm_t(l21, l21)
    l22 = lax.linalg.cholesky(schur, symmetrize_input=False)
    l22 = jnp.tril(l22)
    w2 = jnp.tril(tri_inverse(l22))
    return w1, l21, w2


def solve(parts, right):
    w1, l21, w2 = parts
    half = w1.shape[0]
    y1 = mm(w1, right[:half])
    y2 = mm(w2, right[half:] - mm(l21, y1))
    x2 = cross_rows(w2, y2)
    x1 = cross_rows(w1, y1 - cross_rows(l21, x2))
    return jnp.concatenate([x1, x2], axis=0)


def level_step(height, blocks_rows, factors, solved, gram, identity):
    width = factors.shape[2]
    weight = 1.0 / (2 ** (height + 1) * blocks_rows)
    basis = factors[:, height, :]
    leading = solved[:, :width]
    remaining = solved[:, width:]
    parts = factor(identity + weight * gram)
    if height == LEVELS - 1:
        panel = node_sum(cross_rows(basis, remaining), height)
        update = solve(parts, weight * panel)
    else:
        following = factors[:, height + 1, :]
        head = remaining[:, :width]
        projections = jnp.concatenate(
            [
                cross_rows(basis, head),
                cross_rows(following, leading),
                cross_rows(following, head),
                cross_rows(basis, remaining[:, width:]),
            ],
            axis=1,
        )
        if height == 1:
            split = 512
            panel_a = node_sum(projections[:, :split], height)
            panel_b = node_sum(projections[:, split:], height, order=(1, 0))
            panel = jnp.concatenate([panel_a, panel_b], axis=1)
        else:
            panel = node_sum(projections, height)
        first = solve(parts, weight * panel[:, :width])
        child = panel[:, 2 * width : 3 * width] - mm(panel[:, width : 2 * width], first)
        gram = child + from_partner(child, "leaf", height + 1)
        update = jnp.concatenate([first, solve(parts, weight * panel[:, 3 * width :])], axis=1)
    solved = remaining - mm(leading, update)
    return solved, gram


def shards(blocks, factors, targets):
    block_rows = blocks.shape[0]
    width = factors.shape[2]
    leaf_parts = factor(blocks, symmetrize=False)
    leading = solve(leaf_parts, factors[:, 0, :])
    gram = node_sum(cross_rows(factors[:, 0, :], leading), 0)
    others = jnp.concatenate([factors[:, 1:, :].reshape(block_rows, -1), targets], axis=1)
    solved = jnp.concatenate([leading, solve(leaf_parts, others)], axis=1)
    identity = jnp.eye(width, dtype=jnp.float32)
    for height in range(LEVELS):
        solved, gram = level_step(height, block_rows, factors, solved, gram, identity)
    return (solved[:, :width], solved[:, width:])


def solution(mesh):
    placed = (P(("win", "leaf"), None), P(("win", "leaf"), None, None), P(("win", "leaf"), None))
    return jax.shard_map(
        shards,
        mesh=mesh,
        in_specs=placed,
        out_specs=(P(("win", "leaf"), None), P(("win", "leaf"), None)),
        check_vma=False,
    )
```
